32 devices in a mesh: section: 4 (over y, x), expert: 8 (over z, core).
Axes of the slice: x: 2, y: 2, z: 4, core: 2. Of those that a mesh axis runs over, the one named last changes fastest.
Arguments:
- tokens: bfloat16 [4, 128, 2048], P(None, 'expert'), may hold values from -6 to 6
- norm_gain: float32 [4, 2048], P('section'), may hold values from 0.1 to 1.9
- gate_weight: bfloat16 [4, 16, 2048, 768], P('section', 'expert'), may hold values from -0.125 to 0.125
- up_weight: bfloat16 [4, 16, 2048, 768], P('section', 'expert'), may hold values from -0.125 to 0.125
- down_weight: bfloat16 [4, 16, 768, 2048], P('section', 'expert'), may hold values from -0.21875 to 0.21875
- routes: int32 [4, 4, 128, 8], P('section', None, 'expert'), may hold values from 0 to 15, all different within a row; in each aligned block of 16 rows (0 to 15, 16 to 31, ..., all dimensions but the last counted through in order) at most 12 rows name the same one
- gates: float32 [4, 4, 128, 8], P('section', None, 'expert'), may hold values from 0.1 to 1
Outputs:
- hidden_states: bfloat16 [4, 4, 128, 2048], P('section', None, 'expert')
The draws below stay inside these ranges and needn't reach their ends.
Inputs may be any that keep to these rules, and one draw needn't show every extreme that they name: `routes`: within one section and micro-batch, the 16 tokens of one device name any one expert at most 12 times, a bound that some expert reaches in some of these blocks; the 8 experts of a token differ.
All inputs are finite; a program needn't handle non-finite values.
Results may differ from the reference program's by a relative error of at most 0.012.
Values may be sent and summed in bfloat16 or wider, within the bound.
No kernel may reach another device: no remote copies, remote signals or barrier semaphores. Data moves between devices by JAX's collectives and lax.ppermute only.
A program may use at most 128 MiB of HBM per device.

```python
import math
import jax
import jax.numpy as jnp
import numpy as np
from jax import lax

D = 2048
FE = 768
TOPK = 8
MB = 4
TOK_DEV = 16
EXPERTS = 16
TOKENS = 128
CAP = 12
N_SECTION = 4
N_EXPERT = 8


def shard_levels(stream_key, extent, cuts, least, high):
    def one(position, parts):
        steps = jax.random.uniform(jax.random.fold_in(jax.random.fold_in(stream_key, 6), position), (parts,), jnp.float32, least / len(cuts), high / len(cuts))
        return jnp.repeat(jnp.exp(steps), extent[position] // parts).reshape((-1,) + (1,) * (len(extent) - position - 1))

    level = one(*cuts[0])
    for cut in cuts[1:]:
        level = level * one(*cut)
    return level


def deal_out(key, own, number, rows, count, top, bound, skew):
    order = jax.random.permutation(key, count)
    heavy_load, ordinary = portions_of(count, rows * top, bound, skew, True), portions_of(count, rows * top, bound, skew, False)
    places = jnp.arange(count)

    def named(sizes, turn):
        used = int((sizes > 0).sum())
        fixed = max(1, used // 4)
        shifted = fixed + (places - fixed + turn * (used - fixed)) % max(1, count - fixed)
        return jnp.zeros((count,), jnp.int32).at[order[jnp.where(places < fixed, places, shifted)]].set(jnp.asarray(sizes, jnp.int32))

    sizes = jnp.where(number % 4 == 0, named(heavy_load, number // 4), named(ordinary, number - number // 4 - 1))
    mixed = jax.random.permutation(jax.random.fold_in(own, 3), count)
    donor, sink = mixed[0:count // 2 * 2:2], mixed[1:count // 2 * 2:2]
    margin = jnp.minimum(sizes[donor] - 1, bound - sizes[sink]) // 2
    margin = jnp.where((donor == order[0]) | (sink == order[0]) | (sizes[sink] == 0), 0, jnp.maximum(margin, 0))
    shifted = jax.random.randint(jax.random.fold_in(own, 4), (count // 2,), 0, 1 << 20) % (margin + 1)
    sizes = sizes.at[donor].add(-shifted).at[sink].add(shifted)
    items = jnp.searchsorted(jnp.cumsum(sizes), jnp.arange(rows * top), side="right").astype(jnp.int32)
    table = items.reshape(top, rows).T
    table = table[jax.random.permutation(jax.random.fold_in(own, 1), rows)]
    turn = jax.random.randint(jax.random.fold_in(own, 2), (rows, 1), 0, top)
    return jnp.take_along_axis(table, (jnp.arange(top)[None, :] + turn) % top, axis=1)


def portions_of(count, total, limit, slope, full):
    portions = [(1 << 20) // math.isqrt(rank ** slope) + 1 for rank in range(1, count + 1)]
    largest = limit if full else min(limit, max(-(-total // count), total * portions[0] // sum(portions)))
    least = 1 if total - largest >= count - 1 else 0
    given, surplus = [largest] + [least] * (count - 1), total - largest - least * (count - 1)
    while surplus > 0:
        free = [i for i in range(1, count) if given[i] < largest] or [i for i in range(1, count) if given[i] < limit]
        whole, remaining = sum([portions[i] for i in free]), surplus
        for i in free:
            more = min(limit - given[i], max(1, remaining * portions[i] // whole), surplus)
            given[i] = given[i] + more
            surplus = surplus - more
    return np.array(given)


def centred(rng, dims, deviation, bound, split=(), held_as=jnp.bfloat16):
    result = deviation * jax.random.normal(rng, dims, jnp.float32)
    if split:
        result = result * shard_levels(rng, dims, split, -0.22, 0.18)
    return jnp.clip(result, -bound, bound).astype(held_as)


def setup_inputs(seed: int = 0) -> dict:
    splits = jax.random.split(jax.random.key(seed), 8)
    tokens = centred(splits[0], (MB, TOKENS, D), 1.0, 6.0, ((1, 8),))
    norm_gain = jnp.clip(1.0 + 0.18 * jax.random.normal(splits[1], (N_SECTION, D), jnp.float32), 0.1, 1.9)
    gate_weight = centred(splits[2], (N_SECTION, EXPERTS, D, FE), D ** -0.5, 0.125, ((0, 4), (1, 8)))
    up_weight = centred(splits[3], (N_SECTION, EXPERTS, D, FE), D ** -0.5, 0.125, ((0, 4), (1, 8)))
    down_weight = centred(splits[4], (N_SECTION, EXPERTS, FE, D), FE ** -0.5, 0.21875, ((0, 4), (1, 8)))
    routes_keys = jax.random.split(jax.random.fold_in(splits[5], 1), N_SECTION * MB * TOKENS // TOK_DEV)
    routes_turns = jax.random.permutation(jax.random.fold_in(splits[5], 3), N_SECTION * MB * TOKENS // TOK_DEV)
    routes = jax.vmap(lambda own, number: deal_out(jax.random.fold_in(splits[5], 2), own, number, TOK_DEV, EXPERTS, TOPK, CAP, 2))(routes_keys, routes_turns).reshape((N_SECTION, MB, TOKENS, TOPK))
    gates = jnp.clip(jnp.exp(math.log(1.0) - 2.3025851 * jax.random.uniform(splits[6], (N_SECTION, MB, TOKENS, TOPK), jnp.float32) ** shard_levels(splits[6], (N_SECTION, MB, TOKENS, TOPK), ((0, 4), (2, 8)), -0.2, 0.2)), 0.1, 1.0)
    return {"tokens": tokens, "norm_gain": norm_gain, "gate_weight": gate_weight, "up_weight": up_weight, "down_weight": down_weight, "routes": routes, "gates": gates}


EPSILON = 1e-06

def place_slots(expert_ids, experts):
    onehot = (expert_ids[:, None] == jnp.arange(experts, dtype=jnp.int32)[None, :]).astype(jnp.int32)
    before = jnp.cumsum(onehot, axis=0) - onehot
    return lax.optimization_barrier(jnp.sum(before * onehot, axis=1)).astype(jnp.int32)

def rms_normed(hidden, gain):
    values = hidden.astype(jnp.float32)
    scale = lax.rsqrt(lax.optimization_barrier(jnp.mean(values * values, axis=-1, keepdims=True)) + EPSILON)
    return (values, (values * scale * gain).astype(jnp.bfloat16))

def expert_rows(rows, w_gate, w_up, w_down):
    gate_part = jnp.dot(rows, w_gate, preferred_element_type=jnp.float32)
    up_part = jnp.dot(rows, w_up, preferred_element_type=jnp.float32)
    inner = (jax.nn.silu(gate_part) * up_part).astype(jnp.bfloat16)
    return jnp.dot(inner, w_down, preferred_element_type=jnp.float32).astype(jnp.bfloat16)

def moe_layer(hidden, gain, w_gate, w_up, w_down, expert_ids, gate_values):
    values, normed = rms_normed(hidden, gain)
    blocks = expert_ids.reshape(N_EXPERT, TOK_DEV * TOPK)
    slot_index = jax.vmap(lambda block: place_slots(block, EXPERTS))(blocks).reshape(-1)
    flat_ids = blocks.reshape(-1)
    token_index = jnp.arange(TOKENS * TOPK, dtype=jnp.int32) // TOPK
    source = token_index // TOK_DEV
    buffer = jnp.zeros((EXPERTS, N_EXPERT, CAP, D), jnp.bfloat16)
    buffer = buffer.at[flat_ids, source, slot_index].set(normed[token_index])

    def one_expert(items):
        rows = items[0].reshape(N_EXPERT * CAP, D)
        return expert_rows(rows, items[1], items[2], items[3]).reshape(N_EXPERT, CAP, D)
    results = lax.map(one_expert, (buffer, w_gate, w_up, w_down))
    returned = results[flat_ids, source, slot_index].reshape(TOKENS, TOPK, D)
    weights = gate_values / lax.optimization_barrier(jnp.sum(gate_values, axis=-1, keepdims=True))
    mixed = lax.optimization_barrier(jnp.sum(weights[:, :, None] * returned.astype(jnp.float32), axis=1))
    return (values + mixed).astype(jnp.bfloat16)

def reference(tokens, norm_gain, gate_weight, up_weight, down_weight, routes, gates):
    current = [tokens[batch_index] for batch_index in range(MB)]
    layers = []
    for section in range(N_SECTION):
        produced = []
        for batch_index in range(MB):
            current[batch_index] = moe_layer(current[batch_index], norm_gain[section], gate_weight[section], up_weight[section], down_weight[section], routes[section, batch_index], gates[section, batch_index])
            produced.append(current[batch_index])
        layers.append(jnp.stack(produced))
    return jnp.stack(layers)
```

```python
import jax
import jax.numpy as jnp
from jax import lax
from jax.sharding import PartitionSpec as P

MB = 4


EPSILON = 1e-06


def shifted(array, axis, by):
    count = lax.axis_size(axis)
    pairs = [(i, i + by) for i in range(count) if 0 <= i + by < count]
    return lax.ppermute(array, axis, pairs)


def rms_normed(hidden, gain):
    values = hidden.astype(jnp.float32)
    scale = lax.rsqrt(jnp.mean(values * values, axis=-1, keepdims=True) + EPSILON)
    return (values, (values * scale * gain).astype(jnp.bfloat16))


def route_weights(routes, gates, first_expert, local_experts):
    weights = gates / jnp.sum(gates, axis=-1, keepdims=True)
    mine = first_expert + jnp.arange(local_experts, dtype=jnp.int32)
    hit = routes[..., None] == mine
    return jnp.sum(jnp.where(hit, weights[..., None], 0.0), axis=-2)


def on_device(tokens, norm_gain, gate_weight, up_weight, down_weight, routes, gates):
    sections = lax.axis_size("section")
    section_index = lax.axis_index("section")
    expert_index = lax.axis_index("expert")
    local_experts = gate_weight.shape[1]
    gain = norm_gain[0]
    w_gate = gate_weight[0]
    w_up = up_weight[0]
    w_down = down_weight[0]
    all_routes = lax.all_gather(routes[0], "expert", axis=1, tiled=True)
    all_gates = lax.all_gather(gates[0], "expert", axis=1, tiled=True)
    mixing = route_weights(all_routes, all_gates, expert_index * local_experts, local_experts)
    tok_rows = tokens.shape[1]
    width = tokens.shape[2]
    held = jnp.zeros((tok_rows, width), jnp.bfloat16)
    collected = jnp.zeros((MB, tok_rows, width), jnp.bfloat16)
    for moment in range(MB + sections - 1):
        if moment > 0:
            arrived = shifted(held, "section", 1)
        else:
            arrived = held
        batch_index = moment - section_index
        active = (batch_index >= 0) & (batch_index < MB)
        clipped = jnp.clip(batch_index, 0, MB - 1)
        first_rows = lax.dynamic_index_in_dim(tokens, clipped, 0, keepdims=False)
        incoming = jnp.where(section_index == 0, first_rows, arrived)
        weight = lax.dynamic_index_in_dim(mixing, clipped, 0, keepdims=False)
        values, normed = rms_normed(incoming, gain)
        rows = lax.all_gather(normed, "expert", axis=0, tiled=True)
        gate_part = jnp.einsum("td,edf->etf", rows, w_gate, preferred_element_type=jnp.float32)
        up_part = jnp.einsum("td,edf->etf", rows, w_up, preferred_element_type=jnp.float32)
        inner = (jax.nn.silu(gate_part) * up_part).astype(jnp.bfloat16)
        expert_out = jnp.einsum(
            "etf,efd->etd", inner, w_down, preferred_element_type=jnp.float32
        ).astype(jnp.bfloat16)
        partial = jnp.sum(weight.T[:, :, None] * expert_out.astype(jnp.float32), axis=0)
        mixed = lax.psum_scatter(partial, "expert", scatter_dimension=0, tiled=True)
        produced = (values + mixed).astype(jnp.bfloat16)
        held = jnp.where(active, produced, incoming)
        updated = lax.dynamic_update_index_in_dim(collected, held, clipped, 0)
        collected = jnp.where(active, updated, collected)
    return collected[None]


def solution(mesh):
    placed = (
        P(None, "expert", None),
        P("section", None),
        P("section", "expert", None, None),
        P("section", "expert", None, None),
        P("section", "expert", None, None),
        P("section", None, "expert", None),
        P("section", None, "expert", None),
    )
    return jax.shard_map(
        on_device,
        mesh=mesh,
        in_specs=placed,
        out_specs=P("section", None, "expert", None),
        check_vma=False,
    )
```

```python
import jax
import jax.numpy as jnp
from jax import lax
from jax.sharding import PartitionSpec as P

MB = 4


EPSILON = 1e-06


def shifted(array, axis, by):
    count = lax.axis_size(axis)
    pairs = [(i, i + by) for i in range(count) if 0 <= i + by < count]
    return lax.ppermute(array, axis, pairs)


def scatter_sum(partial, axis):
    count = lax.axis_size(axis)
    index = lax.axis_index(axis)
    blocks = partial.reshape((count, partial.shape[0] // count) + partial.shape[1:])
    total = lax.dynamic_index_in_dim(blocks, index, 0, keepdims=False).astype(jnp.bfloat16).astype(jnp.float32)
    for by in range(1, count):
        piece = lax.dynamic_index_in_dim(blocks, (index + by) % count, 0, keepdims=False)
        pairs = [(i, (i + by) % count) for i in range(count)]
        total = total + lax.ppermute(piece.astype(jnp.bfloat16), axis, pairs).astype(jnp.float32)
    return total


def rms_normed(hidden, gain):
    values = hidden.astype(jnp.float32)
    scale = lax.rsqrt(jnp.mean(values * values, axis=-1, keepdims=True) + EPSILON)
    return (values, (values * scale * gain).astype(jnp.bfloat16))


def route_weights(routes, gates, first_expert, local_experts):
    weights = gates / jnp.sum(gates, axis=-1, keepdims=True)
    mine = first_expert + jnp.arange(local_experts, dtype=jnp.int32)
    hit = routes[..., None] == mine
    return jnp.sum(jnp.where(hit, weights[..., None], 0.0), axis=-2)


def on_device(tokens, norm_gain, gate_weight, up_weight, down_weight, routes, gates):
    sections = lax.axis_size("section")
    section_index = lax.axis_index("section")
    expert_index = lax.axis_index("expert")
    local_experts = gate_weight.shape[1]
    gain = norm_gain[0]
    w_gate = gate_weight[0]
    w_up = up_weight[0]
    w_down = down_weight[0]
    all_routes = lax.all_gather(routes[0], "expert", axis=1, tiled=True)
    all_gates = lax.all_gather(gates[0], "expert", axis=1, tiled=True)
    mixing = route_weights(all_routes, all_gates, expert_index * local_experts, local_experts)
    tok_rows = tokens.shape[1]
    width = tokens.shape[2]
    held = jnp.zeros((tok_rows, width), jnp.bfloat16)
    collected = jnp.zeros((MB, tok_rows, width), jnp.bfloat16)
    for moment in range(MB + sections - 1):
        if moment > 0:
            arrived = shifted(held, "section", 1)
        else:
            arrived = held
        batch_index = moment - section_index
        active = (batch_index >= 0) & (batch_index < MB)
        clipped = jnp.clip(batch_index, 0, MB - 1)
        first_rows = lax.dynamic_index_in_dim(tokens, clipped, 0, keepdims=False)
        incoming = jnp.where(section_index == 0, first_rows, arrived)
        weight = lax.dynamic_index_in_dim(mixing, clipped, 0, keepdims=False)
        values, normed = rms_normed(incoming, gain)
        rows = lax.all_gather(normed, "expert", axis=0, tiled=True)
        gate_part = jnp.einsum("td,edf->etf", rows, w_gate, preferred_element_type=jnp.float32)
        up_part = jnp.einsum("td,edf->etf", rows, w_up, preferred_element_type=jnp.float32)
        inner = (jax.nn.silu(gate_part) * up_part).astype(jnp.bfloat16)
        expert_out = jnp.einsum(
            "etf,efd->etd", inner, w_down, preferred_element_type=jnp.float32
        ).astype(jnp.bfloat16)
        partial = jnp.sum(weight.T[:, :, None] * expert_out.astype(jnp.float32), axis=0)
        mixed = scatter_sum(partial, "expert")
        produced = (values + mixed).astype(jnp.bfloat16)
        held = jnp.where(active, produced, incoming)
        updated = lax.dynamic_update_index_in_dim(collected, held, clipped, 0)
        collected = jnp.where(active, updated, collected)
    return collected[None]


def solution(mesh):
    placed = (
        P(None, "expert", None),
        P("section", None),
        P("section", "expert", None, None),
        P("section", "expert", None, None),
        P("section", "expert", None, None),
        P("section", None, "expert", None),
        P("section", None, "expert", None),
    )
    return jax.shard_map(
        on_device,
        mesh=mesh,
        in_specs=placed,
        out_specs=P("section", None, "expert", None),
        check_vma=False,
    )
```

```python
import jax
import jax.numpy as jnp
from jax import lax
from jax.sharding import PartitionSpec as P

MB = 4


EPSILON = 1e-06


def shifted(array, axis, by):
    count = lax.axis_size(axis)
    pairs = [(i, i + by) for i in range(count) if 0 <= i + by < count]
    return lax.ppermute(array, axis, pairs)


def chip_shift(array, axis, by):
    count = lax.axis_size(axis)
    chips = count // 2
    pairs = [(i, ((i // 2 + by) % chips) * 2 + i % 2) for i in range(count)]
    return lax.ppermute(array, axis, pairs)


def core_swap(array, axis):
    count = lax.axis_size(axis)
    return lax.ppermute(array, axis, [(i, i ^ 1) for i in range(count)])


def gather_blocks(array, axis):
    chips = lax.axis_size(axis) // 2
    own = jnp.stack([array] + [chip_shift(array, axis, k) for k in range(1, chips)])
    return jnp.stack([own, core_swap(own, axis)])


def scatter_blocks(partial, axis):
    chips = lax.axis_size(axis) // 2
    swapped = core_swap(partial[1].astype(jnp.bfloat16), axis)
    chip_sum = partial[0] + swapped.astype(jnp.float32)
    total = chip_sum[0]
    for k in range(1, chips):
        total = total + chip_shift(chip_sum[k].astype(jnp.bfloat16), axis, -k).astype(jnp.float32)
    return total


def rms_normed(hidden, gain):
    values = hidden.astype(jnp.float32)
    scale = lax.rsqrt(jnp.mean(values * values, axis=-1, keepdims=True) + EPSILON)
    return (values, (values * scale * gain).astype(jnp.bfloat16))


def route_table(routes, gates, experts):
    weights = gates / jnp.sum(gates, axis=-1, keepdims=True)
    hit = routes[..., None] == jnp.arange(experts, dtype=jnp.int32)
    return jnp.sum(jnp.where(hit, weights[..., None], 0.0), axis=-2)


def on_device(tokens, norm_gain, gate_weight, up_weight, down_weight, routes, gates):
    devices = lax.axis_size("expert")
    sections = lax.axis_size("section")
    section_index = lax.axis_index("section")
    expert_index = lax.axis_index("expert")
    local_experts = gate_weight.shape[1]
    experts = local_experts * devices
    chips = devices // 2
    gain = norm_gain[0]
    w_gate = gate_weight[0]
    w_up = up_weight[0]
    w_down = down_weight[0]
    tok_rows = tokens.shape[1]
    width = tokens.shape[2]
    table = route_table(routes[0], gates[0], experts)
    table = gather_blocks(table, "expert")
    mine = lax.dynamic_slice_in_dim(table, expert_index * local_experts, local_experts, axis=4)
    mixing = jnp.transpose(mine, (2, 4, 0, 1, 3)).reshape(MB, local_experts, 2 * chips * tok_rows)
    held = jnp.zeros((tok_rows, width), jnp.bfloat16)
    collected = jnp.zeros((MB, tok_rows, width), jnp.bfloat16)
    for moment in range(MB + sections - 1):
        if moment > 0:
            arrived = shifted(held, "section", 1)
        else:
            arrived = held
        batch_index = moment - section_index
        active = (batch_index >= 0) & (batch_index < MB)
        clipped = jnp.clip(batch_index, 0, MB - 1)
        first_rows = lax.dynamic_index_in_dim(tokens, clipped, 0, keepdims=False)
        incoming = jnp.where(section_index == 0, first_rows, arrived)
        weight = lax.dynamic_index_in_dim(mixing, clipped, 0, keepdims=False)
        values, normed = rms_normed(incoming, gain)
        rows = gather_blocks(normed, "expert").reshape(2 * chips * tok_rows, width)
        gate_part = jnp.einsum("td,edf->etf", rows, w_gate, preferred_element_type=jnp.float32)
        up_part = jnp.einsum("td,edf->etf", rows, w_up, preferred_element_type=jnp.float32)
        inner = (jax.nn.silu(gate_part) * up_part * weight[:, :, None]).astype(jnp.bfloat16)
        partial = jnp.einsum("etf,efd->td", inner, w_down, preferred_element_type=jnp.float32)
        mixed = scatter_blocks(partial.reshape(2, chips, tok_rows, width), "expert")
        produced = (values + mixed).astype(jnp.bfloat16)
        held = jnp.where(active, produced, incoming)
        updated = lax.dynamic_update_index_in_dim(collected, held, clipped, 0)
        collected = jnp.where(active, updated, collected)
    return collected[None]


def solution(mesh):
    placed = (
        P(None, "expert", None),
        P("section", None),
        P("section", "expert", None, None),
        P("section", "expert", None, None),
        P("section", "expert", None, None),
        P("section", None, "expert", None),
        P("section", None, "expert", None),
    )
    return jax.shard_map(
        on_device,
        mesh=mesh,
        in_specs=placed,
        out_specs=P("section", None, "expert", None),
        check_vma=False,
    )
```

```python
import jax
import jax.numpy as jnp
from jax import lax
from jax.sharding import PartitionSpec as P

MB = 4


EPSILON = 1e-06


def shifted(array, axis, by):
    count = lax.axis_size(axis)
    pairs = [(i, i + by) for i in range(count) if 0 <= i + by < count]
    return lax.ppermute(array, axis, pairs)


def chip_shift(array, axis, by):
    count = lax.axis_size(axis)
    chips = count // 2
    pairs = [(i, ((i // 2 + by) % chips) * 2 + i % 2) for i in range(count)]
    return lax.ppermute(array, axis, pairs)


def core_swap(array, axis):
    count = lax.axis_size(axis)
    return lax.ppermute(array, axis, [(i, i ^ 1) for i in range(count)])


def gather_blocks(array, axis):
    chips = lax.axis_size(axis) // 2
    own = jnp.stack([array] + [chip_shift(array, axis, k) for k in range(1, chips)])
    return jnp.stack([own, core_swap(own, axis)])


def chip_sums(partial, axis):
    swapped = core_swap(partial[1].astype(jnp.bfloat16), axis)
    return (partial[0] + swapped.astype(jnp.float32)).astype(jnp.bfloat16)


def to_next_section(array, by):
    sections = lax.axis_size("section")
    count = lax.axis_size("expert")
    chips = count // 2
    pairs = [
        (s * count + i, (s + 1) * count + ((i // 2 - by) % chips) * 2 + i % 2)
        for s in range(sections - 1)
        for i in range(count)
    ]
    return lax.ppermute(array, ("section", "expert"), pairs)


def rms_normed(hidden, gain):
    values = hidden.astype(jnp.float32)
    scale = lax.rsqrt(jnp.mean(values * values, axis=-1, keepdims=True) + EPSILON)
    return (values, (values * scale * gain).astype(jnp.bfloat16))


def route_table(routes, gates, experts):
    weights = gates / jnp.sum(gates, axis=-1, keepdims=True)
    hit = routes[..., None] == jnp.arange(experts, dtype=jnp.int32)
    return jnp.sum(jnp.where(hit, weights[..., None], 0.0), axis=-2)


def on_device(tokens, norm_gain, gate_weight, up_weight, down_weight, routes, gates):
    devices = lax.axis_size("expert")
    sections = lax.axis_size("section")
    section_index = lax.axis_index("section")
    expert_index = lax.axis_index("expert")
    local_experts = gate_weight.shape[1]
    experts = local_experts * devices
    chips = devices // 2
    gain = norm_gain[0]
    w_gate = gate_weight[0]
    w_up = up_weight[0]
    w_down = down_weight[0]
    tok_rows = tokens.shape[1]
    width = tokens.shape[2]
    table = route_table(routes[0], gates[0], experts)
    table = gather_blocks(table, "expert")
    mine = lax.dynamic_slice_in_dim(table, expert_index * local_experts, local_experts, axis=4)
    mixing = jnp.transpose(mine, (2, 4, 0, 1, 3)).reshape(MB, local_experts, 2 * chips * tok_rows)
    incoming_next = jnp.zeros((tok_rows, width), jnp.bfloat16)
    collected = jnp.zeros((MB, tok_rows, width), jnp.bfloat16)
    last = MB + sections - 2
    for moment in range(MB + sections - 1):
        batch_index = moment - section_index
        active = (batch_index >= 0) & (batch_index < MB)
        clipped = jnp.clip(batch_index, 0, MB - 1)
        first_rows = lax.dynamic_index_in_dim(tokens, clipped, 0, keepdims=False)
        incoming = jnp.where(section_index == 0, first_rows, incoming_next)
        weight = lax.dynamic_index_in_dim(mixing, clipped, 0, keepdims=False)
        values, normed = rms_normed(incoming, gain)
        if moment < last:
            residual_next = shifted(incoming, "section", 1)
        rows = gather_blocks(normed, "expert").reshape(2 * chips * tok_rows, width)
        gate_part = jnp.einsum("td,edf->etf", rows, w_gate, preferred_element_type=jnp.float32)
        up_part = jnp.einsum("td,edf->etf", rows, w_up, preferred_element_type=jnp.float32)
        inner = (jax.nn.silu(gate_part) * up_part * weight[:, :, None]).astype(jnp.bfloat16)
        partial = jnp.einsum("etf,efd->td", inner, w_down, preferred_element_type=jnp.float32)
        sums = chip_sums(partial.reshape(2, chips, tok_rows, width), "expert")
        total = values + sums[0].astype(jnp.float32)
        for k in range(1, chips):
            total = total + chip_shift(sums[k], "expert", -k).astype(jnp.float32)
        produced = total.astype(jnp.bfloat16)
        updated = lax.dynamic_update_index_in_dim(collected, produced, clipped, 0)
        collected = jnp.where(active, updated, collected)
        if moment < last:
            ahead = residual_next.astype(jnp.float32)
            for k in range(chips):
                ahead = ahead + to_next_section(sums[k], k).astype(jnp.float32)
            incoming_next = ahead.astype(jnp.bfloat16)
    return collected[None]


def solution(mesh):
    placed = (
        P(None, "expert", None),
        P("section", None),
        P("section", "expert", None, None),
        P("section", "expert", None, None),
        P("section", "expert", None, None),
        P("section", None, "expert", None),
        P("section", None, "expert", None),
    )
    return jax.shard_map(
        on_device,
        mesh=mesh,
        in_specs=placed,
        out_specs=P("section", None, "expert", None),
        check_vma=False,
    )
```

```python
import jax
import jax.numpy as jnp
from jax import lax
from jax.sharding import PartitionSpec as P

MB = 4


EPSILON = 1e-06


def shifted(array, axis, by):
    count = lax.axis_size(axis)
    pairs = [(i, i + by) for i in range(count) if 0 <= i + by < count]
    return lax.ppermute(array, axis, pairs)


def exchange_masks(count):
    masks = []
    bit = 1
    while bit < count:
        masks.append(bit)
        bit *= 2
    return masks[1:][::-1] + masks[:1]


def swap(array, axis, mask):
    count = lax.axis_size(axis)
    return lax.ppermute(array, axis, [(i, i ^ mask) for i in range(count)])


def gather_blocks(array, axis):
    blocks = array[None]
    for mask in exchange_masks(lax.axis_size(axis)):
        blocks = jnp.concatenate([blocks, swap(blocks, axis, mask)])
    return blocks


def scatter_blocks(partial, axis):
    blocks = partial
    for mask in exchange_masks(lax.axis_size(axis))[::-1]:
        half = blocks.shape[0] // 2
        blocks = blocks[:half] + swap(blocks[half:].astype(jnp.bfloat16), axis, mask).astype(jnp.float32)
    return blocks[0]


def rms_normed(hidden, gain):
    values = hidden.astype(jnp.float32)
    scale = lax.rsqrt(jnp.mean(values * values, axis=-1, keepdims=True) + EPSILON)
    return (values, (values * scale * gain).astype(jnp.bfloat16))


def route_table(routes, gates, experts):
    weights = gates / jnp.sum(gates, axis=-1, keepdims=True)
    hit = routes[..., None] == jnp.arange(experts, dtype=jnp.int32)
    return jnp.sum(jnp.where(hit, weights[..., None], 0.0), axis=-2)


def on_device(tokens, norm_gain, gate_weight, up_weight, down_weight, routes, gates):
    devices = lax.axis_size("expert")
    sections = lax.axis_size("section")
    section_index = lax.axis_index("section")
    expert_index = lax.axis_index("expert")
    local_experts = gate_weight.shape[1]
    experts = local_experts * devices
    gain = norm_gain[0]
    w_gate = gate_weight[0]
    w_up = up_weight[0]
    w_down = down_weight[0]
    tok_rows = tokens.shape[1]
    width = tokens.shape[2]
    table = route_table(routes[0], gates[0], experts)
    table = gather_blocks(table, "expert")
    mine = lax.dynamic_slice_in_dim(table, expert_index * local_experts, local_experts, axis=3)
    mixing = jnp.transpose(mine, (1, 3, 0, 2)).reshape(MB, local_experts, devices * tok_rows)
    held = jnp.zeros((tok_rows, width), jnp.bfloat16)
    collected = jnp.zeros((MB, tok_rows, width), jnp.bfloat16)
    for moment in range(MB + sections - 1):
        if moment > 0:
            arrived = shifted(held, "section", 1)
        else:
            arrived = held
        batch_index = moment - section_index
        active = (batch_index >= 0) & (batch_index < MB)
        clipped = jnp.clip(batch_index, 0, MB - 1)
        first_rows = lax.dynamic_index_in_dim(tokens, clipped, 0, keepdims=False)
        incoming = jnp.where(section_index == 0, first_rows, arrived)
        weight = lax.dynamic_index_in_dim(mixing, clipped, 0, keepdims=False)
        values, normed = rms_normed(incoming, gain)
        rows = gather_blocks(normed, "expert").reshape(devices * tok_rows, width)
        gate_part = jnp.einsum("td,edf->etf", rows, w_gate, preferred_element_type=jnp.float32)
        up_part = jnp.einsum("td,edf->etf", rows, w_up, preferred_element_type=jnp.float32)
        inner = (jax.nn.silu(gate_part) * up_part * weight[:, :, None]).astype(jnp.bfloat16)
        partial = jnp.einsum("etf,efd->td", inner, w_down, preferred_element_type=jnp.float32)
        mixed = scatter_blocks(partial.reshape(devices, tok_rows, width), "expert")
        produced = (values + mixed).astype(jnp.bfloat16)
        held = jnp.where(active, produced, incoming)
        updated = lax.dynamic_update_index_in_dim(collected, held, clipped, 0)
        collected = jnp.where(active, updated, collected)
    return collected[None]


def solution(mesh):
    placed = (
        P(None, "expert", None),
        P("section", None),
        P("section", "expert", None, None),
        P("section", "expert", None, None),
        P("section", "expert", None, None),
        P("section", None, "expert", None),
        P("section", None, "expert", None),
    )
    return jax.shard_map(
        on_device,
        mesh=mesh,
        in_specs=placed,
        out_specs=P("section", None, "expert", None),
        check_vma=False,
    )
```

```python
import jax
import jax.numpy as jnp
from jax import lax
from jax.sharding import PartitionSpec as P

MB = 4
GROUP = 2


EPSILON = 1e-06


def shifted(array, axis, by):
    count = lax.axis_size(axis)
    pairs = [(i, i + by) for i in range(count) if 0 <= i + by < count]
    return lax.ppermute(array, axis, pairs)


def chip_shift(array, axis, by):
    count = lax.axis_size(axis)
    chips = count // 2
    pairs = [(i, ((i // 2 + by) % chips) * 2 + i % 2) for i in range(count)]
    return lax.ppermute(array, axis, pairs)


def core_swap(array, axis):
    count = lax.axis_size(axis)
    return lax.ppermute(array, axis, [(i, i ^ 1) for i in range(count)])


def gather_blocks(array, axis):
    chips = lax.axis_size(axis) // 2
    own = jnp.stack([array] + [chip_shift(array, axis, k) for k in range(1, chips)])
    return jnp.stack([own, core_swap(own, axis)])


def scatter_blocks(partial, axis):
    chips = lax.axis_size(axis) // 2
    swapped = core_swap(partial[1].astype(jnp.bfloat16), axis)
    chip_sum = partial[0] + swapped.astype(jnp.float32)
    total = chip_sum[0]
    for k in range(1, chips):
        total = total + chip_shift(chip_sum[k].astype(jnp.bfloat16), axis, -k).astype(jnp.float32)
    return total


def rms_normed(hidden, gain):
    values = hidden.astype(jnp.float32)
    scale = lax.rsqrt(jnp.mean(values * values, axis=-1, keepdims=True) + EPSILON)
    return (values, (values * scale * gain).astype(jnp.bfloat16))


def route_table(routes, gates, experts):
    weights = gates / jnp.sum(gates, axis=-1, keepdims=True)
    hit = routes[..., None] == jnp.arange(experts, dtype=jnp.int32)
    return jnp.sum(jnp.where(hit, weights[..., None], 0.0), axis=-2)


def on_device(tokens, norm_gain, gate_weight, up_weight, down_weight, routes, gates):
    devices = lax.axis_size("expert")
    sections = lax.axis_size("section")
    section_index = lax.axis_index("section")
    expert_index = lax.axis_index("expert")
    local_experts = gate_weight.shape[1]
    experts = local_experts * devices
    chips = devices // 2
    gain = norm_gain[0]
    w_gate = gate_weight[0]
    w_up = up_weight[0]
    w_down = down_weight[0]
    tok_rows = tokens.shape[1]
    width = tokens.shape[2]
    table = route_table(routes[0], gates[0], experts)
    table = gather_blocks(table, "expert")
    mine = lax.dynamic_slice_in_dim(table, expert_index * local_experts, local_experts, axis=4)
    mixing = jnp.transpose(mine, (2, 4, 0, 1, 3))
    held = jnp.zeros((GROUP, tok_rows, width), jnp.bfloat16)
    collected = jnp.zeros((MB, tok_rows, width), jnp.bfloat16)
    groups = MB // GROUP
    for moment in range(groups + sections - 1):
        if moment > 0:
            arrived = shifted(held, "section", 1)
        else:
            arrived = held
        group_index = moment - section_index
        active = (group_index >= 0) & (group_index < groups)
        start = jnp.clip(group_index, 0, groups - 1) * GROUP
        first_rows = lax.dynamic_slice_in_dim(tokens, start, GROUP, axis=0)
        incoming = jnp.where(section_index == 0, first_rows, arrived)
        weight = lax.dynamic_slice_in_dim(mixing, start, GROUP, axis=0)
        weight = jnp.transpose(weight, (1, 2, 3, 0, 4)).reshape(local_experts, -1)
        values, normed = rms_normed(incoming, gain)
        rows = gather_blocks(normed, "expert").reshape(-1, width)
        gate_part = jnp.einsum("td,edf->etf", rows, w_gate, preferred_element_type=jnp.float32)
        up_part = jnp.einsum("td,edf->etf", rows, w_up, preferred_element_type=jnp.float32)
        inner = (jax.nn.silu(gate_part) * up_part * weight[:, :, None]).astype(jnp.bfloat16)
        partial = jnp.einsum("etf,efd->td", inner, w_down, preferred_element_type=jnp.float32)
        mixed = scatter_blocks(partial.reshape(2, chips, GROUP, tok_rows, width), "expert")
        produced = (values + mixed).astype(jnp.bfloat16)
        held = jnp.where(active, produced, incoming)
        updated = lax.dynamic_update_slice_in_dim(collected, held, start, axis=0)
        collected = jnp.where(active, updated, collected)
    return collected[None]


def solution(mesh):
    placed = (
        P(None, "expert", None),
        P("section", None),
        P("section", "expert", None, None),
        P("section", "expert", None, None),
        P("section", "expert", None, None),
        P("section", None, "expert", None),
        P("section", None, "expert", None),
    )
    return jax.shard_map(
        on_device,
        mesh=mesh,
        in_specs=placed,
        out_specs=P("section", None, "expert", None),
        check_vma=False,
    )
```

```python
import jax
import jax.numpy as jnp
from jax import lax
from jax.sharding import PartitionSpec as P
from jax.experimental import pallas as pl
from jax.experimental.pallas import tpu as pltpu

MB = 4


EPSILON = 1e-06


def shifted(array, axis, by):
    count = lax.axis_size(axis)
    pairs = [(i, i + by) for i in range(count) if 0 <= i + by < count]
    return lax.ppermute(array, axis, pairs)


def chip_shift(array, axis, by):
    count = lax.axis_size(axis)
    chips = count // 2
    pairs = [(i, ((i // 2 + by) % chips) * 2 + i % 2) for i in range(count)]
    return lax.ppermute(array, axis, pairs)


def core_swap(array, axis):
    count = lax.axis_size(axis)
    return lax.ppermute(array, axis, [(i, i ^ 1) for i in range(count)])


def gather_blocks(array, axis):
    chips = lax.axis_size(axis) // 2
    own = jnp.stack([array] + [chip_shift(array, axis, k) for k in range(1, chips)])
    return jnp.stack([own, core_swap(own, axis)])


def scatter_blocks(partial, axis):
    chips = lax.axis_size(axis) // 2
    swapped = core_swap(partial[1].astype(jnp.bfloat16), axis)
    chip_sum = partial[0] + swapped.astype(jnp.float32)
    total = chip_sum[0]
    for k in range(1, chips):
        total = total + chip_shift(chip_sum[k].astype(jnp.bfloat16), axis, -k).astype(jnp.float32)
    return total


def expert_kernel(rows_ref, gate_ref, up_ref, down_ref, weight_ref, out_ref):
    first = (pl.program_id(0) == 0) & (pl.program_id(1) == 0)

    @pl.when(first)
    def _():
        out_ref[...] = jnp.zeros_like(out_ref)

    rows = rows_ref[...]
    gate_part = jnp.dot(rows, gate_ref[...], preferred_element_type=jnp.float32)
    up_part = jnp.dot(rows, up_ref[...], preferred_element_type=jnp.float32)
    inner = (jax.nn.silu(gate_part) * up_part * weight_ref[...]).astype(jnp.bfloat16)
    out_ref[...] += jnp.dot(inner, down_ref[...], preferred_element_type=jnp.float32)


def experts_mixed(rows, w_gate, w_up, w_down, weight, chunk=256):
    count, width = rows.shape
    local, _, hidden = w_gate.shape
    chunks = hidden // chunk
    return pl.pallas_call(
        expert_kernel,
        grid=(local, chunks),
        in_specs=[
            pl.BlockSpec((count, width), lambda e, f: (0, 0)),
            pl.BlockSpec((None, width, chunk), lambda e, f: (e, 0, f)),
            pl.BlockSpec((None, width, chunk), lambda e, f: (e, 0, f)),
            pl.BlockSpec((None, chunk, width), lambda e, f: (e, f, 0)),
            pl.BlockSpec((None, count, 1), lambda e, f: (e, 0, 0)),
        ],
        out_specs=pl.BlockSpec((count, width), lambda e, f: (0, 0)),
        out_shape=jax.ShapeDtypeStruct((count, width), jnp.float32),
        compiler_params=pltpu.CompilerParams(dimension_semantics=("arbitrary", "arbitrary")),
    )(rows, w_gate, w_up, w_down, weight[:, :, None])


def rms_normed(hidden, gain):
    values = hidden.astype(jnp.float32)
    scale = lax.rsqrt(jnp.mean(values * values, axis=-1, keepdims=True) + EPSILON)
    return (values, (values * scale * gain).astype(jnp.bfloat16))


def route_table(routes, gates, experts):
    weights = gates / jnp.sum(gates, axis=-1, keepdims=True)
    hit = routes[..., None] == jnp.arange(experts, dtype=jnp.int32)
    return jnp.sum(jnp.where(hit, weights[..., None], 0.0), axis=-2)


def on_device(tokens, norm_gain, gate_weight, up_weight, down_weight, routes, gates):
    devices = lax.axis_size("expert")
    sections = lax.axis_size("section")
    section_index = lax.axis_index("section")
    expert_index = lax.axis_index("expert")
    local_experts = gate_weight.shape[1]
    experts = local_experts * devices
    chips = devices // 2
    gain = norm_gain[0]
    w_gate = gate_weight[0]
    w_up = up_weight[0]
    w_down = down_weight[0]
    tok_rows = tokens.shape[1]
    width = tokens.shape[2]
    table = route_table(routes[0], gates[0], experts)
    table = gather_blocks(table, "expert")
    mine = lax.dynamic_slice_in_dim(table, expert_index * local_experts, local_experts, axis=4)
    mixing = jnp.transpose(mine, (2, 4, 0, 1, 3)).reshape(MB, local_experts, 2 * chips * tok_rows)
    held = jnp.zeros((tok_rows, width), jnp.bfloat16)
    collected = jnp.zeros((MB, tok_rows, width), jnp.bfloat16)
    for moment in range(MB + sections - 1):
        if moment > 0:
            arrived = shifted(held, "section", 1)
        else:
            arrived = held
        batch_index = moment - section_index
        active = (batch_index >= 0) & (batch_index < MB)
        clipped = jnp.clip(batch_index, 0, MB - 1)
        first_rows = lax.dynamic_index_in_dim(tokens, clipped, 0, keepdims=False)
        incoming = jnp.where(section_index == 0, first_rows, arrived)
        weight = lax.dynamic_index_in_dim(mixing, clipped, 0, keepdims=False)
        values, normed = rms_normed(incoming, gain)
        rows = gather_blocks(normed, "expert").reshape(2 * chips * tok_rows, width)
        partial = experts_mixed(rows, w_gate, w_up, w_down, weight)
        mixed = scatter_blocks(partial.reshape(2, chips, tok_rows, width), "expert")
        produced = (values + mixed).astype(jnp.bfloat16)
        held = jnp.where(active, produced, incoming)
        updated = lax.dynamic_update_index_in_dim(collected, held, clipped, 0)
        collected = jnp.where(active, updated, collected)
    return collected[None]


def solution(mesh):
    placed = (
        P(None, "expert", None),
        P("section", None),
        P("section", "expert", None, None),
        P("section", "expert", None, None),
        P("section", "expert", None, None),
        P("section", None, "expert", None),
        P("section", None, "expert", None),
    )
    return jax.shard_map(
        on_device,
        mesh=mesh,
        in_specs=placed,
        out_specs=P("section", None, "expert", None),
        check_vma=False,
    )
```

```python
import jax
import jax.numpy as jnp
from jax import lax
from jax.sharding import PartitionSpec as P
from jax.experimental import pallas as pl
from jax.experimental.pallas import tpu as pltpu

MB = 4


EPSILON = 1e-06


def shifted(array, axis, by):
    count = lax.axis_size(axis)
    pairs = [(i, i + by) for i in range(count) if 0 <= i + by < count]
    return lax.ppermute(array, axis, pairs)


def chip_shift(array, axis, by):
    count = lax.axis_size(axis)
    chips = count // 2
    pairs = [(i, ((i // 2 + by) % chips) * 2 + i % 2) for i in range(count)]
    return lax.ppermute(array, axis, pairs)


def core_swap(array, axis):
    count = lax.axis_size(axis)
    return lax.ppermute(array, axis, [(i, i ^ 1) for i in range(count)])


def gather_blocks(array, axis):
    chips = lax.axis_size(axis) // 2
    own = jnp.stack([array] + [chip_shift(array, axis, k) for k in range(1, chips)])
    return jnp.stack([own, core_swap(own, axis)])


def scatter_blocks(partial, axis):
    chips = lax.axis_size(axis) // 2
    swapped = core_swap(partial[1].astype(jnp.bfloat16), axis)
    chip_sum = partial[0] + swapped.astype(jnp.float32)
    total = chip_sum[0]
    for k in range(1, chips):
        total = total + chip_shift(chip_sum[k].astype(jnp.bfloat16), axis, -k).astype(jnp.float32)
    return total


def expert_kernel(rows_ref, gate_ref, up_ref, down_ref, weight_ref, out_ref):
    first = (pl.program_id(0) == 0) & (pl.program_id(1) == 0)

    @pl.when(first)
    def _():
        out_ref[...] = jnp.zeros_like(out_ref)

    rows = rows_ref[...]
    gate_part = jnp.dot(rows, gate_ref[...], preferred_element_type=jnp.float32)
    up_part = jnp.dot(rows, up_ref[...], preferred_element_type=jnp.float32)
    inner = (jax.nn.silu(gate_part) * up_part * weight_ref[...]).astype(jnp.bfloat16)
    out_ref[...] += jnp.dot(inner, down_ref[...], preferred_element_type=jnp.float32)


def experts_mixed(rows, w_gate, w_up, w_down, weight, chunk=768):
    count, width = rows.shape
    local, _, hidden = w_gate.shape
    chunks = hidden // chunk
    return pl.pallas_call(
        expert_kernel,
        grid=(local, chunks),
        in_specs=[
            pl.BlockSpec((count, width), lambda e, f: (0, 0)),
            pl.BlockSpec((None, width, chunk), lambda e, f: (e, 0, f)),
            pl.BlockSpec((None, width, chunk), lambda e, f: (e, 0, f)),
            pl.BlockSpec((None, chunk, width), lambda e, f: (e, f, 0)),
            pl.BlockSpec((None, count, 1), lambda e, f: (e, 0, 0)),
        ],
        out_specs=pl.BlockSpec((count, width), lambda e, f: (0, 0)),
        out_shape=jax.ShapeDtypeStruct((count, width), jnp.float32),
        compiler_params=pltpu.CompilerParams(dimension_semantics=("arbitrary", "arbitrary")),
    )(rows, w_gate, w_up, w_down, weight[:, :, None])


def rms_normed(hidden, gain):
    values = hidden.astype(jnp.float32)
    scale = lax.rsqrt(jnp.mean(values * values, axis=-1, keepdims=True) + EPSILON)
    return (values, (values * scale * gain).astype(jnp.bfloat16))


def route_table(routes, gates, experts):
    weights = gates / jnp.sum(gates, axis=-1, keepdims=True)
    hit = routes[..., None] == jnp.arange(experts, dtype=jnp.int32)
    return jnp.sum(jnp.where(hit, weights[..., None], 0.0), axis=-2)


def on_device(tokens, norm_gain, gate_weight, up_weight, down_weight, routes, gates):
    devices = lax.axis_size("expert")
    sections = lax.axis_size("section")
    section_index = lax.axis_index("section")
    expert_index = lax.axis_index("expert")
    local_experts = gate_weight.shape[1]
    experts = local_experts * devices
    chips = devices // 2
    gain = norm_gain[0]
    w_gate = gate_weight[0]
    w_up = up_weight[0]
    w_down = down_weight[0]
    tok_rows = tokens.shape[1]
    width = tokens.shape[2]
    table = route_table(routes[0], gates[0], experts)
    table = gather_blocks(table, "expert")
    mine = lax.dynamic_slice_in_dim(table, expert_index * local_experts, local_experts, axis=4)
    mixing = jnp.transpose(mine, (2, 4, 0, 1, 3)).reshape(MB, local_experts, 2 * chips * tok_rows)
    held = jnp.zeros((tok_rows, width), jnp.bfloat16)
    collected = jnp.zeros((MB, tok_rows, width), jnp.bfloat16)
    for moment in range(MB + sections - 1):
        if moment > 0:
            arrived = shifted(held, "section", 1)
        else:
            arrived = held
        batch_index = moment - section_index
        active = (batch_index >= 0) & (batch_index < MB)
        clipped = jnp.clip(batch_index, 0, MB - 1)
        first_rows = lax.dynamic_index_in_dim(tokens, clipped, 0, keepdims=False)
        incoming = jnp.where(section_index == 0, first_rows, arrived)
        weight = lax.dynamic_index_in_dim(mixing, clipped, 0, keepdims=False)
        values, normed = rms_normed(incoming, gain)
        rows = gather_blocks(normed, "expert").reshape(2 * chips * tok_rows, width)
        partial = experts_mixed(rows, w_gate, w_up, w_down, weight)
        mixed = scatter_blocks(partial.reshape(2, chips, tok_rows, width), "expert")
        produced = (values + mixed).astype(jnp.bfloat16)
        held = jnp.where(active, produced, incoming)
        updated = lax.dynamic_update_index_in_dim(collected, held, clipped, 0)
        collected = jnp.where(active, updated, collected)
    return collected[None]


def solution(mesh):
    placed = (
        P(None, "expert", None),
        P("section", None),
        P("section", "expert", None, None),
        P("section", "expert", None, None),
        P("section", "expert", None, None),
        P("section", None, "expert", None),
        P("section", None, "expert", None),
    )
    return jax.shard_map(
        on_device,
        mesh=mesh,
        in_specs=placed,
        out_specs=P("section", None, "expert", None),
        check_vma=False,
    )
```

```python
import jax
import jax.numpy as jnp
from jax import lax
from jax.sharding import PartitionSpec as P

MB = 4


EPSILON = 1e-06


def shifted(array, axis, by):
    count = lax.axis_size(axis)
    pairs = [(i, i + by) for i in range(count) if 0 <= i + by < count]
    return lax.ppermute(array, axis, pairs)


def chip_shift(array, axis, by):
    count = lax.axis_size(axis)
    chips = count // 2
    pairs = [(i, ((i // 2 + by) % chips) * 2 + i % 2) for i in range(count)]
    return lax.ppermute(array, axis, pairs)


def core_swap(array, axis):
    count = lax.axis_size(axis)
    return lax.ppermute(array, axis, [(i, i ^ 1) for i in range(count)])


def gather_blocks(array, axis):
    chips = lax.axis_size(axis) // 2
    own = jnp.stack([array] + [chip_shift(array, axis, k) for k in range(1, chips)])
    return jnp.stack([own, core_swap(own, axis)])


def scatter_blocks(partial, axis):
    chips = lax.axis_size(axis) // 2
    swapped = core_swap(partial[1].astype(jnp.bfloat16), axis)
    chip_sum = partial[0] + swapped.astype(jnp.float32)
    total = chip_sum[0]
    for k in range(1, chips):
        total = total + chip_shift(chip_sum[k].astype(jnp.bfloat16), axis, -k).astype(jnp.float32)
    return total


def to_next_section(array, by):
    sections = lax.axis_size("section")
    count = lax.axis_size("expert")
    chips = count // 2
    pairs = [
        (s * count + i, ((s + 1) % sections) * count + ((i // 2 + by) % chips) * 2 + i % 2)
        for s in range(sections)
        for i in range(count)
    ]
    return lax.ppermute(array, ("section", "expert"), pairs)


def rms_normed(hidden, gain):
    values = hidden.astype(jnp.float32)
    scale = lax.rsqrt(jnp.mean(values * values, axis=-1, keepdims=True) + EPSILON)
    return (values, (values * scale * gain).astype(jnp.bfloat16))


def route_table(routes, gates, experts):
    weights = gates / jnp.sum(gates, axis=-1, keepdims=True)
    hit = routes[..., None] == jnp.arange(experts, dtype=jnp.int32)
    return jnp.sum(jnp.where(hit, weights[..., None], 0.0), axis=-2)


def on_device(tokens, norm_gain, gate_weight, up_weight, down_weight, routes, gates):
    devices = lax.axis_size("expert")
    sections = lax.axis_size("section")
    section_index = lax.axis_index("section")
    expert_index = lax.axis_index("expert")
    local_experts = gate_weight.shape[1]
    experts = local_experts * devices
    chips = devices // 2
    gain = norm_gain[0]
    w_gate = gate_weight[0]
    w_up = up_weight[0]
    w_down = down_weight[0]
    tok_rows = tokens.shape[1]
    width = tokens.shape[2]
    table = route_table(routes[0], gates[0], experts)
    table = gather_blocks(table, "expert")
    mine = lax.dynamic_slice_in_dim(table, expert_index * local_experts, local_experts, axis=4)
    mixing = jnp.transpose(mine, (2, 4, 0, 1, 3)).reshape(MB, local_experts, 2 * chips * tok_rows)
    collected = jnp.zeros((MB, tok_rows, width), jnp.bfloat16)
    blocks = gather_blocks(tokens[0], "expert")[0]
    last = MB + sections - 2
    for moment in range(MB + sections - 1):
        batch_index = moment - section_index
        active = (batch_index >= 0) & (batch_index < MB)
        clipped = jnp.clip(batch_index, 0, MB - 1)
        weight = lax.dynamic_index_in_dim(mixing, clipped, 0, keepdims=False)
        rows = jnp.stack([blocks, core_swap(blocks, "expert")])
        values, normed = rms_normed(rows, gain)
        rows = normed.reshape(2 * chips * tok_rows, width)
        gate_part = jnp.einsum("td,edf->etf", rows, w_gate, preferred_element_type=jnp.float32)
        up_part = jnp.einsum("td,edf->etf", rows, w_up, preferred_element_type=jnp.float32)
        inner = (jax.nn.silu(gate_part) * up_part * weight[:, :, None]).astype(jnp.bfloat16)
        partial = jnp.einsum("etf,efd->td", inner, w_down, preferred_element_type=jnp.float32)
        mixed = scatter_blocks(partial.reshape(2, chips, tok_rows, width), "expert")
        produced = (values[0, 0] + mixed).astype(jnp.bfloat16)
        updated = lax.dynamic_update_index_in_dim(collected, produced, clipped, 0)
        collected = jnp.where(active, updated, collected)
        if moment < last:
            upcoming = lax.dynamic_index_in_dim(tokens, min(moment + 1, MB - 1), 0, keepdims=False)
            outgoing = jnp.where(section_index == sections - 1, upcoming, produced)
            blocks = jnp.stack([to_next_section(outgoing, k) for k in range(chips)])
    return collected[None]


def solution(mesh):
    placed = (
        P(None, "expert", None),
        P("section", None),
        P("section", "expert", None, None),
        P("section", "expert", None, None),
        P("section", "expert", None, None),
        P("section", None, "expert", None),
        P("section", None, "expert", None),
    )
    return jax.shard_map(
        on_device,
        mesh=mesh,
        in_specs=placed,
        out_specs=P("section", None, "expert", None),
        check_vma=False,
    )
```

```python
import jax
import jax.numpy as jnp
from jax import lax
from jax.sharding import PartitionSpec as P

MB = 4


EPSILON = 1e-06


def shifted(array, axis, by):
    count = lax.axis_size(axis)
    pairs = [(i, i + by) for i in range(count) if 0 <= i + by < count]
    return lax.ppermute(array, axis, pairs)


def chip_shift(array, axis, by):
    count = lax.axis_size(axis)
    chips = count // 2
    pairs = [(i, ((i // 2 + by) % chips) * 2 + i % 2) for i in range(count)]
    return lax.ppermute(array, axis, pairs)


def core_swap(array, axis):
    count = lax.axis_size(axis)
    return lax.ppermute(array, axis, [(i, i ^ 1) for i in range(count)])


def gather_blocks(array, axis):
    chips = lax.axis_size(axis) // 2
    own = jnp.stack([array] + [chip_shift(array, axis, k) for k in range(1, chips)])
    return jnp.stack([own, core_swap(own, axis)])


def scatter_blocks(partial, axis):
    chips = lax.axis_size(axis) // 2
    swapped = core_swap(partial[1].astype(jnp.bfloat16), axis)
    chip_sum = partial[0] + swapped.astype(jnp.float32)
    total = chip_sum[0]
    for k in range(1, chips):
        total = total + chip_shift(chip_sum[k].astype(jnp.bfloat16), axis, -k).astype(jnp.float32)
    return total


def to_next_section(array, by):
    sections = lax.axis_size("section")
    count = lax.axis_size("expert")
    chips = count // 2
    pairs = [
        (s * count + i, ((s + 1) % sections) * count + ((i // 2 + by) % chips) * 2 + i % 2)
        for s in range(sections)
        for i in range(count)
    ]
    return lax.ppermute(array, ("section", "expert"), pairs)


def rms_normed(hidden, gain):
    values = hidden.astype(jnp.float32)
    scale = lax.rsqrt(jnp.mean(values * values, axis=-1, keepdims=True) + EPSILON)
    return (values, (values * scale * gain).astype(jnp.bfloat16))


def route_table(routes, gates, experts):
    weights = gates / jnp.sum(gates, axis=-1, keepdims=True)
    hit = routes[..., None] == jnp.arange(experts, dtype=jnp.int32)
    return jnp.sum(jnp.where(hit, weights[..., None], 0.0), axis=-2)


def on_device(tokens, norm_gain, gate_weight, up_weight, down_weight, routes, gates):
    devices = lax.axis_size("expert")
    sections = lax.axis_size("section")
    section_index = lax.axis_index("section")
    expert_index = lax.axis_index("expert")
    local_experts = gate_weight.shape[1]
    experts = local_experts * devices
    chips = devices // 2
    gain = norm_gain[0]
    w_gate = gate_weight[0]
    w_up = up_weight[0]
    w_down = down_weight[0]
    tok_rows = tokens.shape[1]
    width = tokens.shape[2]
    table = route_table(routes[0], gates[0], experts)
    high = table.astype(jnp.bfloat16)
    low = (table - high.astype(jnp.float32)).astype(jnp.bfloat16)
    packed = jnp.concatenate([high.reshape(-1), low.reshape(-1)])
    extra = -(-packed.shape[0] // width)
    packed = jnp.pad(packed, (0, extra * width - packed.shape[0])).reshape(extra, width)
    first = gather_blocks(jnp.concatenate([tokens[0], packed]), "expert")
    first_rows = first[:, :, :tok_rows]
    packed = first[:, :, tok_rows:].reshape(2, chips, extra * width)[:, :, : 2 * table.size]
    table = packed[:, :, : table.size].astype(jnp.float32) + packed[:, :, table.size :].astype(jnp.float32)
    table = table.reshape((2, chips) + high.shape)
    mine = lax.dynamic_slice_in_dim(table, expert_index * local_experts, local_experts, axis=4)
    mixing = jnp.transpose(mine, (2, 4, 0, 1, 3)).reshape(MB, local_experts, 2 * chips * tok_rows)
    collected = jnp.zeros((MB, tok_rows, width), jnp.bfloat16)
    last = MB + sections - 2
    for moment in range(MB + sections - 1):
        batch_index = moment - section_index
        active = (batch_index >= 0) & (batch_index < MB)
        clipped = jnp.clip(batch_index, 0, MB - 1)
        weight = lax.dynamic_index_in_dim(mixing, clipped, 0, keepdims=False)
        if moment == 0:
            rows = first_rows
        else:
            rows = jnp.stack([blocks, core_swap(blocks, "expert")])
        values, normed = rms_normed(rows, gain)
        rows = normed.reshape(2 * chips * tok_rows, width)
        gate_part = jnp.einsum("td,edf->etf", rows, w_gate, preferred_element_type=jnp.float32)
        up_part = jnp.einsum("td,edf->etf", rows, w_up, preferred_element_type=jnp.float32)
        inner = (jax.nn.silu(gate_part) * up_part * weight[:, :, None]).astype(jnp.bfloat16)
        partial = jnp.einsum("etf,efd->td", inner, w_down, preferred_element_type=jnp.float32)
        mixed = scatter_blocks(partial.reshape(2, chips, tok_rows, width), "expert")
        produced = (values[0, 0] + mixed).astype(jnp.bfloat16)
        updated = lax.dynamic_update_index_in_dim(collected, produced, clipped, 0)
        collected = jnp.where(active, updated, collected)
        if moment < last:
            upcoming = lax.dynamic_index_in_dim(tokens, min(moment + 1, MB - 1), 0, keepdims=False)
            outgoing = jnp.where(section_index == sections - 1, upcoming, produced)
            blocks = jnp.stack([to_next_section(outgoing, k) for k in range(chips)])
    return collected[None]


def solution(mesh):
    placed = (
        P(None, "expert", None),
        P("section", None),
        P("section", "expert", None, None),
        P("section", "expert", None, None),
        P("section", "expert", None, None),
        P("section", None, "expert", None),
        P("section", None, "expert", None),
    )
    return jax.shard_map(
        on_device,
        mesh=mesh,
        in_specs=placed,
        out_specs=P("section", None, "expert", None),
        check_vma=False,
    )
```

```python
import jax
import jax.numpy as jnp
from jax import lax
from jax.sharding import PartitionSpec as P

MB = 4


EPSILON = 1e-06


def shifted(array, axis, by):
    count = lax.axis_size(axis)
    pairs = [(i, i + by) for i in range(count) if 0 <= i + by < count]
    return lax.ppermute(array, axis, pairs)


def chip_shift(array, axis, by):
    count = lax.axis_size(axis)
    chips = count // 2
    pairs = [(i, ((i // 2 + by) % chips) * 2 + i % 2) for i in range(count)]
    return lax.ppermute(array, axis, pairs)


def core_swap(array, axis):
    count = lax.axis_size(axis)
    return lax.ppermute(array, axis, [(i, i ^ 1) for i in range(count)])


def gather_blocks(array, axis):
    chips = lax.axis_size(axis) // 2
    own = jnp.stack([array] + [chip_shift(array, axis, k) for k in range(1, chips)])
    return jnp.stack([own, core_swap(own, axis)])


def scatter_blocks(partial, axis):
    chips = lax.axis_size(axis) // 2
    swapped = core_swap(partial[1].astype(jnp.bfloat16), axis)
    chip_sum = partial[0] + swapped.astype(jnp.float32)
    total = chip_sum[0]
    for k in range(1, chips):
        total = total + chip_shift(chip_sum[k].astype(jnp.bfloat16), axis, -k).astype(jnp.float32)
    return total


def to_next_section(array, by):
    sections = lax.axis_size("section")
    count = lax.axis_size("expert")
    chips = count // 2
    pairs = [
        (s * count + i, ((s + 1) % sections) * count + ((i // 2 + by) % chips) * 2 + i % 2)
        for s in range(sections)
        for i in range(count)
    ]
    return lax.ppermute(array, ("section", "expert"), pairs)


def rms_normed(hidden, gain):
    values = hidden.astype(jnp.float32)
    scale = lax.rsqrt(jnp.mean(values * values, axis=-1, keepdims=True) + EPSILON)
    return (values, (values * scale * gain).astype(jnp.bfloat16))


def route_table(routes, gates, experts):
    weights = gates / jnp.sum(gates, axis=-1, keepdims=True)
    hit = routes[..., None] == jnp.arange(experts, dtype=jnp.int32)
    return jnp.sum(jnp.where(hit, weights[..., None], 0.0), axis=-2)


def on_device(tokens, norm_gain, gate_weight, up_weight, down_weight, routes, gates):
    devices = lax.axis_size("expert")
    sections = lax.axis_size("section")
    section_index = lax.axis_index("section")
    expert_index = lax.axis_index("expert")
    local_experts = gate_weight.shape[1]
    experts = local_experts * devices
    chips = devices // 2
    gain = norm_gain[0]
    w_gate = gate_weight[0]
    w_up = up_weight[0]
    w_down = down_weight[0]
    tok_rows = tokens.shape[1]
    width = tokens.shape[2]
    table = route_table(routes[0], gates[0], experts)
    high = table.astype(jnp.bfloat16)
    low = (table - high.astype(jnp.float32)).astype(jnp.bfloat16)
    packed = jnp.concatenate([high.reshape(-1), low.reshape(-1)])
    extra = -(-packed.shape[0] // width)
    packed = jnp.pad(packed, (0, extra * width - packed.shape[0])).reshape(extra, width)
    first = gather_blocks(jnp.concatenate([tokens[0], packed]), "expert")
    first_rows = first[:, :, :tok_rows]
    packed = first[:, :, tok_rows:].reshape(2, chips, extra * width)[:, :, : 2 * table.size]
    table = packed[:, :, : table.size].astype(jnp.float32) + packed[:, :, table.size :].astype(jnp.float32)
    table = table.reshape((2, chips) + high.shape)
    mine = lax.dynamic_slice_in_dim(table, expert_index * local_experts, local_experts, axis=4)
    mixing = jnp.transpose(mine, (2, 4, 0, 1, 3)).reshape(MB, local_experts, 2 * chips * tok_rows)
    collected = jnp.zeros((MB, tok_rows, width), jnp.bfloat16)
    last = MB + sections - 2
    for moment in range(MB + sections - 1):
        batch_index = moment - section_index
        active = (batch_index >= 0) & (batch_index < MB)
        clipped = jnp.clip(batch_index, 0, MB - 1)
        weight = lax.dynamic_index_in_dim(mixing, clipped, 0, keepdims=False)
        if moment == 0:
            rows = first_rows
        else:
            rows = jnp.stack([blocks, core_swap(blocks, "expert")])
        values, normed = rms_normed(rows, gain)
        rows = normed.reshape(2 * chips * tok_rows, width)
        gate_part = jnp.einsum("td,edf->etf", rows, w_gate, preferred_element_type=jnp.float32)
        up_part = jnp.einsum("td,edf->etf", rows, w_up, preferred_element_type=jnp.float32)
        inner = (jax.nn.silu(gate_part) * up_part * weight[:, :, None]).astype(jnp.bfloat16)
        partial = jnp.einsum("etf,efd->td", inner, w_down, preferred_element_type=jnp.float32)
        mixed = scatter_blocks(partial.reshape(2, chips, tok_rows, width), "expert")
        produced = (values[0, 0] + mixed).astype(jnp.bfloat16)
        updated = lax.dynamic_update_index_in_dim(collected, produced, clipped, 0)
        collected = jnp.where(active, updated, collected)
        if moment < last:
            upcoming = lax.dynamic_index_in_dim(tokens, min(moment + 1, MB - 1), 0, keepdims=False)
            outgoing = jnp.where(section_index == sections - 1, upcoming, produced)
            sent = {k: to_next_section(outgoing, k) for k in range(chips - 1, -1, -1)}
            blocks = jnp.stack([sent[k] for k in range(chips)])
    return collected[None]


def solution(mesh):
    placed = (
        P(None, "expert", None),
        P("section", None),
        P("section", "expert", None, None),
        P("section", "expert", None, None),
        P("section", "expert", None, None),
        P("section", None, "expert", None),
        P("section", None, "expert", None),
    )
    return jax.shard_map(
        on_device,
        mesh=mesh,
        in_specs=placed,
        out_specs=P("section", None, "expert", None),
        check_vma=False,
    )
```

```python
import jax
import jax.numpy as jnp
from jax import lax
from jax.sharding import PartitionSpec as P

MB = 4


EPSILON = 1e-06


def shifted(array, axis, by):
    count = lax.axis_size(axis)
    pairs = [(i, i + by) for i in range(count) if 0 <= i + by < count]
    return lax.ppermute(array, axis, pairs)


def chip_swap(array, axis, mask):
    count = lax.axis_size(axis)
    pairs = [(i, ((i // 2) ^ mask) * 2 + i % 2) for i in range(count)]
    return lax.ppermute(array, axis, pairs)


def core_swap(array, axis):
    count = lax.axis_size(axis)
    return lax.ppermute(array, axis, [(i, i ^ 1) for i in range(count)])


def gather_blocks(array, axis):
    chips = lax.axis_size(axis) // 2
    own = jnp.stack([array] + [chip_swap(array, axis, k) for k in range(1, chips)])
    return jnp.stack([own, core_swap(own, axis)])


def scatter_blocks(partial, axis):
    chips = lax.axis_size(axis) // 2
    swapped = core_swap(partial[1].astype(jnp.bfloat16), axis)
    chip_sum = partial[0] + swapped.astype(jnp.float32)
    total = chip_sum[0]
    for k in range(1, chips):
        total = total + chip_swap(chip_sum[k].astype(jnp.bfloat16), axis, k).astype(jnp.float32)
    return total


def to_next_section(array, by):
    sections = lax.axis_size("section")
    count = lax.axis_size("expert")
    chips = count // 2
    pairs = [
        (s * count + i, ((s + 1) % sections) * count + ((i // 2) ^ by) * 2 + i % 2)
        for s in range(sections)
        for i in range(count)
    ]
    return lax.ppermute(array, ("section", "expert"), pairs)


def rms_normed(hidden, gain):
    values = hidden.astype(jnp.float32)
    scale = lax.rsqrt(jnp.mean(values * values, axis=-1, keepdims=True) + EPSILON)
    return (values, (values * scale * gain).astype(jnp.bfloat16))


def route_table(routes, gates, experts):
    weights = gates / jnp.sum(gates, axis=-1, keepdims=True)
    hit = routes[..., None] == jnp.arange(experts, dtype=jnp.int32)
    return jnp.sum(jnp.where(hit, weights[..., None], 0.0), axis=-2)


def on_device(tokens, norm_gain, gate_weight, up_weight, down_weight, routes, gates):
    devices = lax.axis_size("expert")
    sections = lax.axis_size("section")
    section_index = lax.axis_index("section")
    expert_index = lax.axis_index("expert")
    local_experts = gate_weight.shape[1]
    experts = local_experts * devices
    chips = devices // 2
    gain = norm_gain[0]
    w_gate = gate_weight[0]
    w_up = up_weight[0]
    w_down = down_weight[0]
    tok_rows = tokens.shape[1]
    width = tokens.shape[2]
    table = route_table(routes[0], gates[0], experts)
    high = table.astype(jnp.bfloat16)
    low = (table - high.astype(jnp.float32)).astype(jnp.bfloat16)
    packed = jnp.concatenate([high.reshape(-1), low.reshape(-1)])
    extra = -(-packed.shape[0] // width)
    packed = jnp.pad(packed, (0, extra * width - packed.shape[0])).reshape(extra, width)
    first = gather_blocks(jnp.concatenate([tokens[0], packed]), "expert")
    first_rows = first[:, :, :tok_rows]
    packed = first[:, :, tok_rows:].reshape(2, chips, extra * width)[:, :, : 2 * table.size]
    table = packed[:, :, : table.size].astype(jnp.float32) + packed[:, :, table.size :].astype(jnp.float32)
    table = table.reshape((2, chips) + high.shape)
    mine = lax.dynamic_slice_in_dim(table, expert_index * local_experts, local_experts, axis=4)
    mixing = jnp.transpose(mine, (2, 4, 0, 1, 3)).reshape(MB, local_experts, 2 * chips * tok_rows)
    collected = jnp.zeros((MB, tok_rows, width), jnp.bfloat16)
    last = MB + sections - 2
    for moment in range(MB + sections - 1):
        batch_index = moment - section_index
        active = (batch_index >= 0) & (batch_index < MB)
        clipped = jnp.clip(batch_index, 0, MB - 1)
        weight = lax.dynamic_index_in_dim(mixing, clipped, 0, keepdims=False)
        if moment == 0:
            rows = first_rows
        else:
            rows = jnp.stack([blocks, core_swap(blocks, "expert")])
        values, normed = rms_normed(rows, gain)
        rows = normed.reshape(2 * chips * tok_rows, width)
        gate_part = jnp.einsum("td,edf->etf", rows, w_gate, preferred_element_type=jnp.float32)
        up_part = jnp.einsum("td,edf->etf", rows, w_up, preferred_element_type=jnp.float32)
        inner = (jax.nn.silu(gate_part) * up_part * weight[:, :, None]).astype(jnp.bfloat16)
        partial = jnp.einsum("etf,efd->td", inner, w_down, preferred_element_type=jnp.float32)
        mixed = scatter_blocks(partial.reshape(2, chips, tok_rows, width), "expert")
        produced = (values[0, 0] + mixed).astype(jnp.bfloat16)
        updated = lax.dynamic_update_index_in_dim(collected, produced, clipped, 0)
        collected = jnp.where(active, updated, collected)
        if moment < last:
            upcoming = lax.dynamic_index_in_dim(tokens, min(moment + 1, MB - 1), 0, keepdims=False)
            outgoing = jnp.where(section_index == sections - 1, upcoming, produced)
            sent = {k: to_next_section(outgoing, k) for k in range(chips - 1, -1, -1)}
            blocks = jnp.stack([sent[k] for k in range(chips)])
    return collected[None]


def solution(mesh):
    placed = (
        P(None, "expert", None),
        P("section", None),
        P("section", "expert", None, None),
        P("section", "expert", None, None),
        P("section", "expert", None, None),
        P("section", None, "expert", None),
        P("section", None, "expert", None),
    )
    return jax.shard_map(
        on_device,
        mesh=mesh,
        in_specs=placed,
        out_specs=P("section", None, "expert", None),
        check_vma=False,
    )
```

```python
import jax
import jax.numpy as jnp
from jax import lax
from jax.sharding import PartitionSpec as P

MB = 4


EPSILON = 1e-06


def shifted(array, axis, by):
    count = lax.axis_size(axis)
    pairs = [(i, i + by) for i in range(count) if 0 <= i + by < count]
    return lax.ppermute(array, axis, pairs)


def chip_swap(array, axis, mask):
    count = lax.axis_size(axis)
    pairs = [(i, ((i // 2) ^ mask) * 2 + i % 2) for i in range(count)]
    return lax.ppermute(array, axis, pairs)


def core_swap(array, axis):
    count = lax.axis_size(axis)
    return lax.ppermute(array, axis, [(i, i ^ 1) for i in range(count)])


def gather_blocks(array, axis):
    chips = lax.axis_size(axis) // 2
    own = jnp.stack([array] + [chip_swap(array, axis, k) for k in range(1, chips)])
    return jnp.stack([own, core_swap(own, axis)])


def scatter_blocks(partial, axis):
    chips = lax.axis_size(axis) // 2
    swapped = core_swap(partial[1].astype(jnp.bfloat16), axis)
    chip_sum = partial[0] + swapped.astype(jnp.float32)
    total = chip_sum[0]
    for k in range(1, chips):
        total = total + chip_swap(chip_sum[k].astype(jnp.bfloat16), axis, k).astype(jnp.float32)
    return total


def to_next_section(array, by):
    sections = lax.axis_size("section")
    count = lax.axis_size("expert")
    chips = count // 2
    pairs = [
        (s * count + i, ((s + 1) % sections) * count + ((i // 2) ^ by) * 2 + i % 2)
        for s in range(sections)
        for i in range(count)
    ]
    return lax.ppermute(array, ("section", "expert"), pairs)


def rms_normed(hidden, gain):
    values = hidden.astype(jnp.float32)
    scale = lax.rsqrt(jnp.mean(values * values, axis=-1, keepdims=True) + EPSILON)
    return (values, (values * scale * gain).astype(jnp.bfloat16))


def route_table(routes, gates, experts):
    weights = gates / jnp.sum(gates, axis=-1, keepdims=True)
    hit = routes[..., None] == jnp.arange(experts, dtype=jnp.int32)
    return jnp.sum(jnp.where(hit, weights[..., None], 0.0), axis=-2)


def on_device(tokens, norm_gain, gate_weight, up_weight, down_weight, routes, gates):
    devices = lax.axis_size("expert")
    sections = lax.axis_size("section")
    section_index = lax.axis_index("section")
    expert_index = lax.axis_index("expert")
    local_experts = gate_weight.shape[1]
    experts = local_experts * devices
    chips = devices // 2
    gain = norm_gain[0]
    w_gate_up = jnp.concatenate([gate_weight[0], up_weight[0]]).transpose(1, 0, 2)
    w_down = down_weight[0]
    tok_rows = tokens.shape[1]
    width = tokens.shape[2]
    table = route_table(routes[0], gates[0], experts)
    high = table.astype(jnp.bfloat16)
    low = (table - high.astype(jnp.float32)).astype(jnp.bfloat16)
    packed = jnp.concatenate([high.reshape(-1), low.reshape(-1)])
    extra = -(-packed.shape[0] // width)
    packed = jnp.pad(packed, (0, extra * width - packed.shape[0])).reshape(extra, width)
    first = gather_blocks(jnp.concatenate([tokens[0], packed]), "expert")
    first_rows = first[:, :, :tok_rows]
    packed = first[:, :, tok_rows:].reshape(2, chips, extra * width)[:, :, : 2 * table.size]
    table = packed[:, :, : table.size].astype(jnp.float32) + packed[:, :, table.size :].astype(jnp.float32)
    table = table.reshape((2, chips) + high.shape)
    mine = lax.dynamic_slice_in_dim(table, expert_index * local_experts, local_experts, axis=4)
    mixing = jnp.transpose(mine, (2, 4, 0, 1, 3)).reshape(MB, local_experts, 2 * chips * tok_rows)
    collected = jnp.zeros((MB, tok_rows, width), jnp.bfloat16)
    last = MB + sections - 2
    for moment in range(MB + sections - 1):
        batch_index = moment - section_index
        active = (batch_index >= 0) & (batch_index < MB)
        clipped = jnp.clip(batch_index, 0, MB - 1)
        weight = lax.dynamic_index_in_dim(mixing, clipped, 0, keepdims=False)
        if moment == 0:
            rows = first_rows
        else:
            rows = jnp.stack([blocks, core_swap(blocks, "expert")])
        values, normed = rms_normed(rows, gain)
        rows = normed.reshape(2 * chips * tok_rows, width)
        both = jnp.einsum("td,def->tef", rows, w_gate_up, preferred_element_type=jnp.float32)
        gate_part = both[:, :local_experts]
        up_part = both[:, local_experts:]
        inner = (jax.nn.silu(gate_part) * up_part * weight.T[:, :, None]).astype(jnp.bfloat16)
        partial = jnp.einsum("tef,efd->td", inner, w_down, preferred_element_type=jnp.float32)
        mixed = scatter_blocks(partial.reshape(2, chips, tok_rows, width), "expert")
        produced = (values[0, 0] + mixed).astype(jnp.bfloat16)
        updated = lax.dynamic_update_index_in_dim(collected, produced, clipped, 0)
        collected = jnp.where(active, updated, collected)
        if moment < last:
            upcoming = lax.dynamic_index_in_dim(tokens, min(moment + 1, MB - 1), 0, keepdims=False)
            outgoing = jnp.where(section_index == sections - 1, upcoming, produced)
            sent = {k: to_next_section(outgoing, k) for k in range(chips - 1, -1, -1)}
            blocks = jnp.stack([sent[k] for k in range(chips)])
    return collected[None]


def solution(mesh):
    placed = (
        P(None, "expert", None),
        P("section", None),
        P("section", "expert", None, None),
        P("section", "expert", None, None),
        P("section", "expert", None, None),
        P("section", None, "expert", None),
        P("section", None, "expert", None),
    )
    return jax.shard_map(
        on_device,
        mesh=mesh,
        in_specs=placed,
        out_specs=P("section", None, "expert", None),
        check_vma=False,
    )
```

```python
import jax
import jax.numpy as jnp
from jax import lax
from jax.sharding import PartitionSpec as P

MB = 4


EPSILON = 1e-06


def shifted(array, axis, by):
    count = lax.axis_size(axis)
    pairs = [(i, i + by) for i in range(count) if 0 <= i + by < count]
    return lax.ppermute(array, axis, pairs)


def chip_swap(array, axis, mask):
    count = lax.axis_size(axis)
    pairs = [(i, ((i // 2) ^ mask) * 2 + i % 2) for i in range(count)]
    return lax.ppermute(array, axis, pairs)


def core_swap(array, axis):
    count = lax.axis_size(axis)
    return lax.ppermute(array, axis, [(i, i ^ 1) for i in range(count)])


def gather_blocks(array, axis):
    chips = lax.axis_size(axis) // 2
    own = jnp.stack([array] + [chip_swap(array, axis, k) for k in range(1, chips)])
    return jnp.stack([own, core_swap(own, axis)])


def scatter_blocks(partial, axis):
    chips = lax.axis_size(axis) // 2
    swapped = core_swap(partial[1].astype(jnp.bfloat16), axis)
    chip_sum = partial[0] + swapped.astype(jnp.float32)
    total = chip_sum[0]
    for k in range(1, chips):
        total = total + chip_swap(chip_sum[k].astype(jnp.bfloat16), axis, k).astype(jnp.float32)
    return total


def to_next_section(array, by):
    sections = lax.axis_size("section")
    count = lax.axis_size("expert")
    chips = count // 2
    pairs = [
        (s * count + i, ((s + 1) % sections) * count + ((i // 2) ^ by) * 2 + i % 2)
        for s in range(sections)
        for i in range(count)
    ]
    return lax.ppermute(array, ("section", "expert"), pairs)


def rms_normed(hidden, gain):
    values = hidden.astype(jnp.float32)
    scale = lax.rsqrt(jnp.mean(values * values, axis=-1, keepdims=True) + EPSILON)
    return (values, (values * scale * gain).astype(jnp.bfloat16))


def route_table(routes, gates, experts):
    weights = gates / jnp.sum(gates, axis=-1, keepdims=True)
    hit = routes[..., None] == jnp.arange(experts, dtype=jnp.int32)
    return jnp.sum(jnp.where(hit, weights[..., None], 0.0), axis=-2)


def on_device(tokens, norm_gain, gate_weight, up_weight, down_weight, routes, gates):
    devices = lax.axis_size("expert")
    sections = lax.axis_size("section")
    section_index = lax.axis_index("section")
    expert_index = lax.axis_index("expert")
    local_experts = gate_weight.shape[1]
    experts = local_experts * devices
    chips = devices // 2
    gain = norm_gain[0]
    w_gate_up = jnp.concatenate([gate_weight[0], up_weight[0]]).transpose(1, 0, 2)
    w_down = down_weight[0]
    tok_rows = tokens.shape[1]
    width = tokens.shape[2]
    table = route_table(routes[0], gates[0], experts)
    high = table.astype(jnp.bfloat16)
    low = (table - high.astype(jnp.float32)).astype(jnp.bfloat16)
    packed = jnp.concatenate([high.reshape(-1), low.reshape(-1)])
    extra = -(-packed.shape[0] // width)
    packed = jnp.pad(packed, (0, extra * width - packed.shape[0])).reshape(extra, width)
    first = gather_blocks(jnp.concatenate([tokens[0], packed]), "expert")
    first_rows = first[:, :, :tok_rows]
    packed = first[:, :, tok_rows:].reshape(2, chips, extra * width)[:, :, : 2 * table.size]
    table = packed[:, :, : table.size].astype(jnp.float32) + packed[:, :, table.size :].astype(jnp.float32)
    table = table.reshape((2, chips) + high.shape)
    mine = lax.dynamic_slice_in_dim(table, expert_index * local_experts, local_experts, axis=4)
    mixing = jnp.transpose(mine, (2, 4, 0, 1, 3)).reshape(MB, local_experts, 2 * chips * tok_rows)
    collected = jnp.zeros((MB, tok_rows, width), jnp.bfloat16)
    last = MB + sections - 2
    for moment in range(MB + sections - 1):
        batch_index = moment - section_index
        active = (batch_index >= 0) & (batch_index < MB)
        clipped = jnp.clip(batch_index, 0, MB - 1)
        weight = lax.dynamic_index_in_dim(mixing, clipped, 0, keepdims=False)
        if moment == 0:
            rows = first_rows
        else:
            rows = jnp.stack([blocks, core_swap(blocks, "expert")])
        values, normed = rms_normed(rows, gain)
        rows = normed.reshape(2 * chips * tok_rows, width)
        both = jnp.einsum("td,def->tef", rows, w_gate_up, preferred_element_type=jnp.float32)
        gate_part = both[:, :local_experts]
        up_part = both[:, local_experts:]
        inner = (jax.nn.silu(gate_part) * up_part * weight.T[:, :, None]).astype(jnp.bfloat16)
        partial = jnp.dot(
            inner.reshape(inner.shape[0], -1), w_down.reshape(-1, width), preferred_element_type=jnp.float32
        )
        mixed = scatter_blocks(partial.reshape(2, chips, tok_rows, width), "expert")
        produced = (values[0, 0] + mixed).astype(jnp.bfloat16)
        updated = lax.dynamic_update_index_in_dim(collected, produced, clipped, 0)
        collected = jnp.where(active, updated, collected)
        if moment < last:
            upcoming = lax.dynamic_index_in_dim(tokens, min(moment + 1, MB - 1), 0, keepdims=False)
            outgoing = jnp.where(section_index == sections - 1, upcoming, produced)
            sent = {k: to_next_section(outgoing, k) for k in range(chips - 1, -1, -1)}
            blocks = jnp.stack([sent[k] for k in range(chips)])
    return collected[None]


def solution(mesh):
    placed = (
        P(None, "expert", None),
        P("section", None),
        P("section", "expert", None, None),
        P("section", "expert", None, None),
        P("section", "expert", None, None),
        P("section", None, "expert", None),
        P("section", None, "expert", None),
    )
    return jax.shard_map(
        on_device,
        mesh=mesh,
        in_specs=placed,
        out_specs=P("section", None, "expert", None),
        check_vma=False,
    )
```
